256 devices in a mesh: seq: 64 (over y, x_lo, z), dp: 4 (over x_hi, core).
Axes of the slice: x: 4 (x_hi: 2, x_lo: 2; x = x_hi * 2 + x_lo), y: 4, z: 8, core: 2. Of those that a mesh axis runs over, the one named last changes fastest.
Arguments:
- inputs: float32 [4, 32768, 256], P('dp', 'seq'), may hold values from -6 to 6
- out_cotangent: float32 [4, 32768, 256], P('dp', 'seq'), may hold values from -6 to 6
- skip_cotangent: float32 [4, 32768, 256], P('dp', 'seq'), may hold values from -6 to 6
- convolution_weight: float32 [2, 512, 1024], replicated, may hold values from -0.25 to 0.25
- convolution_bias: float32 [2, 1024], replicated, may hold values from -3 to 3
- output_weight: float32 [2, 512, 512], replicated, may hold values from -0.25 to 0.25
Outputs:
- input_grad: float32 [4, 32768, 256], P('dp', 'seq')
- conv_grad: float32 [1024, 1024], P(('seq', 'dp'))
- out_grad: float32 [1024, 512], P(('seq', 'dp'))
- bias_grad: float32 [2048], P(('seq', 'dp'))
The draws below stay inside these ranges and needn't reach their ends.
All inputs are finite; a program needn't handle non-finite values.
Results may differ from the reference program's by a relative error of at most 0.00025.
Values sent between devices are 32-bit elements; how exact they have to be, the bound alone decides.
No kernel may reach another device: no remote copies, remote signals or barrier semaphores. Data moves between devices by JAX's collectives and lax.ppermute only.
A program may use at most 128 MiB of HBM per device.

```python
import math
import jax
import jax.numpy as jnp
from jax import lax

R = 256
G = 512
LAYERS = 2
FIRST_DILATION = 256
SECOND_DILATION = 512
LENGTH = 32768
SEQS = 4


def shard_levels(stream_key, shape, pieces, least, high):
    level, own = 1.0, jax.random.fold_in(stream_key, 6)
    for dim, shards_of in pieces:
        heights = jnp.exp(jax.random.uniform(jax.random.fold_in(own, dim), (shards_of,), jnp.float32, least / len(pieces), high / len(pieces)))
        level = level * jnp.repeat(heights, shape[dim] // shards_of).reshape([-1 if axis == dim else 1 for axis in range(len(shape))])
    return level


def scatter_about(stream_key, extent, width, limit, split=(), dtype=jnp.bfloat16):
    factor_of = shard_levels(stream_key, extent, split, -0.22, 0.18) if split else 1.0
    values = jax.random.normal(stream_key, extent, jnp.float32) * width * factor_of
    return jnp.minimum(jnp.maximum(values, -limit), limit).astype(dtype)


def setup_inputs(seed: int = 0) -> dict:
    splits = jax.random.split(jax.random.key(seed), 7)
    return {
        "inputs": scatter_about(splits[0], (SEQS, LENGTH, R), 1.0, 6.0, ((0, 4), (1, 64)), jnp.float32),
        "out_cotangent": scatter_about(splits[1], (SEQS, LENGTH, R), 1.0, 6.0, ((0, 4), (1, 64)), jnp.float32),
        "skip_cotangent": scatter_about(splits[2], (SEQS, LENGTH, R), 1.0, 6.0, ((0, 4), (1, 64)), jnp.float32),
        "convolution_weight": scatter_about(splits[3], (LAYERS, 2 * R, 2 * G), (2 * R) ** -0.5, 0.25, (), jnp.float32),
        "convolution_bias": scatter_about(splits[4], (LAYERS, 2 * G), 0.5, 3.0, (), jnp.float32),
        "output_weight": scatter_about(splits[5], (LAYERS, G, 2 * R), G ** -0.5, 0.25, (), jnp.float32),
    }


def matmul(left, right):
    return jnp.dot(left, right, precision=lax.Precision.HIGHEST, preferred_element_type=jnp.float32)

def past_rows(values, shift_by):
    zeros = jnp.zeros((shift_by, values.shape[1]), jnp.float32)
    return jnp.concatenate([zeros, values[:-shift_by]], axis=0)

def future_rows(values, shift_by):
    zeros = jnp.zeros((shift_by, values.shape[1]), jnp.float32)
    return jnp.concatenate([values[shift_by:], zeros], axis=0)

def layer_forward_step(values, weight, bias, shift_by):
    earlier = past_rows(values, shift_by)
    joined = jnp.concatenate([earlier, values], axis=1)
    mixed = matmul(joined, weight) + bias
    tanh_part = jnp.tanh(mixed[:, :G])
    sigm_part = jax.nn.sigmoid(mixed[:, G:])
    return (joined, tanh_part, sigm_part, tanh_part * sigm_part)

def layer_backward_step(joined, tanh_part, sigm_part, hidden, weight, out_w, carried_state, skip_cotangent_rows, shift_by):
    outer = jnp.concatenate([carried_state, skip_cotangent_rows], axis=1)
    dhidden = matmul(outer, out_w.T)
    dfilter = dhidden * sigm_part * (1.0 - tanh_part * tanh_part)
    dgate = dhidden * tanh_part * sigm_part * (1.0 - sigm_part)
    dmixed = jnp.concatenate([dfilter, dgate], axis=1)
    out_t = matmul(outer.T, hidden)
    conv_g = matmul(joined.T, dmixed)
    bias_g = lax.optimization_barrier(jnp.sum(dmixed, axis=0))
    back = matmul(dmixed, weight.T)
    new_carried = carried_state + back[:, R:] + future_rows(back[:, :R], shift_by)
    return (new_carried, conv_g, out_t, bias_g)

def one_sequence(packed, convolution_weight, convolution_bias, output_weight):
    start_row, output_cotangent_rows, skip_cotangent_rows = (packed[0], packed[1], packed[2])
    first_joined, first_tanh, first_sigmoid, first_hidden = layer_forward_step(start_row, convolution_weight[0], convolution_bias[0], FIRST_DILATION)
    second_layer = start_row + matmul(first_hidden, output_weight[0][:, :R])
    second_joined, second_tanh, second_sigmoid, second_hidden = layer_forward_step(second_layer, convolution_weight[1], convolution_bias[1], SECOND_DILATION)
    carried_state, second_conv_output, second_output, second_bias = layer_backward_step(second_joined, second_tanh, second_sigmoid, second_hidden, convolution_weight[1], output_weight[1], output_cotangent_rows, skip_cotangent_rows, SECOND_DILATION)
    carried_state, first_conv_output, first_output, first_bias = layer_backward_step(first_joined, first_tanh, first_sigmoid, first_hidden, convolution_weight[0], output_weight[0], carried_state, skip_cotangent_rows, FIRST_DILATION)
    return (carried_state, jnp.concatenate([first_conv_output, second_conv_output], axis=0), jnp.concatenate([first_output, second_output], axis=0), jnp.concatenate([first_bias, second_bias], axis=0))

def reference(inputs, out_cotangent, skip_cotangent, convolution_weight, convolution_bias, output_weight):
    packed = jnp.stack([inputs, out_cotangent, skip_cotangent], axis=1)
    grads, conv_all, out_all, bias_all = lax.map(lambda item: one_sequence(item, convolution_weight, convolution_bias, output_weight), packed)
    factor = 1.0 / math.sqrt(SEQS * LENGTH)
    return (grads, lax.optimization_barrier(jnp.sum(conv_all, axis=0)) * factor, lax.optimization_barrier(jnp.sum(out_all, axis=0)) * factor, lax.optimization_barrier(jnp.sum(bias_all, axis=0)) * factor)
```

```python
import math

import jax
import jax.numpy as jnp
from jax import lax
from jax.sharding import PartitionSpec as P


SEQ_AXES = ("y", "xl", "z")


def from_behind(block, axis, distance):
    devices = range(lax.axis_size(axis))
    route = [(i - distance, i) for i in devices if i - distance in devices]
    return lax.ppermute(block, axis, route)


def matmul(left, right):
    return jnp.dot(left, right, precision=lax.Precision.HIGHEST, preferred_element_type=jnp.float32)


def contract(left, right, left_dim, right_dim):
    return lax.dot_general(
        left,
        right,
        (((left_dim,), (right_dim,)), ((), ())),
        precision=lax.Precision.HIGHEST,
        preferred_element_type=jnp.float32,
    )


def layer_forward_step(earlier, values, weight, bias):
    joined = jnp.concatenate([earlier, values], axis=1)
    mixed = matmul(joined, weight) + bias
    width = weight.shape[1] // 2
    tanh_part = jnp.tanh(mixed[:, :width])
    sigm_part = jax.nn.sigmoid(mixed[:, width:])
    return (joined, tanh_part, sigm_part, tanh_part * sigm_part)


def layer_backward_step(
    joined, tanh_part, sigm_part, hidden, weight, out_w, carried_state, skip_cotangent_rows
):
    channels = carried_state.shape[1]
    outer = jnp.concatenate([carried_state, skip_cotangent_rows], axis=1)
    dhidden = contract(outer, out_w, 1, 1)
    dfilter = dhidden * sigm_part * (1.0 - tanh_part * tanh_part)
    dgate = dhidden * tanh_part * sigm_part * (1.0 - sigm_part)
    dmixed = jnp.concatenate([dfilter, dgate], axis=1)
    out_t = contract(outer, hidden, 0, 0)
    conv_g = contract(joined, dmixed, 0, 0)
    bias_g = jnp.sum(dmixed, axis=0)
    back = contract(dmixed, weight, 1, 1)
    return (back[:, :channels], back[:, channels:], conv_g, out_t, bias_g)


def local(
    inputs, out_cotangent, skip_cotangent, convolution_weight, convolution_bias, output_weight
):
    start_row = inputs[0]
    output_cotangent_rows = out_cotangent[0]
    skip_cotangent_rows = skip_cotangent[0]
    rows, channels = start_row.shape
    half = rows // 2
    tail = from_behind(start_row[rows - half :], SEQ_AXES, 1)
    earlier1 = jnp.concatenate([tail, start_row[: rows - half]], axis=0)
    first_joined, first_tanh, first_sigmoid, first_hidden = layer_forward_step(
        earlier1, start_row, convolution_weight[0], convolution_bias[0]
    )
    second_layer = start_row + matmul(first_hidden, output_weight[0][:, :channels])
    earlier2 = from_behind(second_layer, SEQ_AXES, 1)
    second_joined, second_tanh, second_sigmoid, second_hidden = layer_forward_step(
        earlier2, second_layer, convolution_weight[1], convolution_bias[1]
    )
    past2, local2, second_conv_output, second_output, second_bias = layer_backward_step(
        second_joined,
        second_tanh,
        second_sigmoid,
        second_hidden,
        convolution_weight[1],
        output_weight[1],
        output_cotangent_rows,
        skip_cotangent_rows,
    )
    carried_state = output_cotangent_rows + local2 + from_behind(past2, SEQ_AXES, -1)
    past1, local1, first_conv_output, first_output, first_bias = layer_backward_step(
        first_joined,
        first_tanh,
        first_sigmoid,
        first_hidden,
        convolution_weight[0],
        output_weight[0],
        carried_state,
        skip_cotangent_rows,
    )
    rim_rows = from_behind(past1[:half], SEQ_AXES, -1)
    input_grad = carried_state + local1 + jnp.concatenate([past1[half:], rim_rows], axis=0)
    seq_axes, dp_axes = SEQ_AXES, ("xh", "c")
    devices = lax.axis_size(seq_axes) * lax.axis_size(dp_axes)
    factor = 1.0 / math.sqrt(rows * devices)
    conv_terms = jnp.concatenate([first_conv_output, second_conv_output], axis=0)
    out_terms = jnp.concatenate([first_output, second_output], axis=0)
    bias_terms = jnp.concatenate([first_bias, second_bias], axis=0) * factor
    conv_rows, out_rows = conv_terms.shape[0] // devices, out_terms.shape[0] // devices
    packed = jnp.concatenate(
        [conv_terms.reshape(devices, -1), out_terms.reshape(devices, -1)], axis=1
    )
    width = packed.shape[1]
    sizes = [lax.axis_size(a) for a in seq_axes + dp_axes]
    packed = packed.reshape(*sizes, width).transpose(4, 2, 0, 3, 1, 5)
    packed = packed.reshape(devices * 8, width // 8)
    summed = lax.psum_scatter(packed, RING_ORDER, scatter_dimension=0, tiled=True).reshape(-1) * factor
    split = conv_rows * conv_terms.shape[1]
    conv_grad = summed[:split].reshape(conv_rows, -1)
    out_grad = summed[split:].reshape(out_rows, -1)
    bias_grad = lax.psum_scatter(bias_terms, seq_axes + dp_axes, scatter_dimension=0, tiled=True)
    return (input_grad[None], conv_grad, out_grad, bias_grad)


RING_ORDER = ("c", "z", "y", "xh", "xl")


def solution(mesh):
    fine = jax.sharding.Mesh(mesh.devices.reshape(4, 2, 8, 2, 2), ("y", "xl", "z", "xh", "c"))
    rows_spec = P(("xh", "c"), ("y", "xl", "z"), None)
    owner = ("y", "xl", "z", "xh", "c")
    return jax.shard_map(
        local,
        mesh=fine,
        in_specs=(rows_spec, rows_spec, rows_spec, P(), P(), P()),
        out_specs=(rows_spec, P(owner, None), P(owner, None), P(owner)),
        check_vma=False,
    )
```

```python
import math

import jax
import jax.numpy as jnp
from jax import lax
from jax.sharding import PartitionSpec as P


SEQ_AXES = ("y", "xl", "z")
DP_AXES = ("xh", "c")


def reduce_rows(block, axis):
    parts = lax.axis_size(axis)
    block = block.reshape(parts, block.shape[0] // parts, block.shape[1])
    return lax.all_to_all(block, axis, 0, 0, tiled=True).sum(axis=0)


def reduce_to_owner(packed):
    rows, width = packed.shape
    halves = lax.all_to_all(packed.reshape(rows, 2, width // 2), "c", 1, 1, tiled=True)
    block = halves.sum(axis=1)
    for axis in ("y", "xl", "z", "xh"):
        block = reduce_rows(block, axis)
    return lax.all_to_all(block, "c", 0, 1, tiled=True)


def from_behind(block, axis, distance):
    devices = range(lax.axis_size(axis))
    route = [(i - distance, i) for i in devices if i - distance in devices]
    return lax.ppermute(block, axis, route)


def matmul(left, right):
    return jnp.dot(left, right, precision=lax.Precision.HIGHEST, preferred_element_type=jnp.float32)


def contract(left, right, left_dim, right_dim):
    return lax.dot_general(
        left,
        right,
        (((left_dim,), (right_dim,)), ((), ())),
        precision=lax.Precision.HIGHEST,
        preferred_element_type=jnp.float32,
    )


def layer_forward_step(earlier, values, weight, bias):
    joined = jnp.concatenate([earlier, values], axis=1)
    mixed = matmul(joined, weight) + bias
    width = weight.shape[1] // 2
    tanh_part = jnp.tanh(mixed[:, :width])
    sigm_part = jax.nn.sigmoid(mixed[:, width:])
    return (joined, tanh_part, sigm_part, tanh_part * sigm_part)


def layer_backward_step(
    joined, tanh_part, sigm_part, hidden, weight, out_w, carried_state, skip_cotangent_rows
):
    channels = carried_state.shape[1]
    outer = jnp.concatenate([carried_state, skip_cotangent_rows], axis=1)
    dhidden = contract(outer, out_w, 1, 1)
    dfilter = dhidden * sigm_part * (1.0 - tanh_part * tanh_part)
    dgate = dhidden * tanh_part * sigm_part * (1.0 - sigm_part)
    dmixed = jnp.concatenate([dfilter, dgate], axis=1)
    out_t = contract(outer, hidden, 0, 0)
    conv_g = contract(joined, dmixed, 0, 0)
    bias_g = jnp.sum(dmixed, axis=0)
    back = contract(dmixed, weight, 1, 1)
    return (back[:, :channels], back[:, channels:], conv_g, out_t, bias_g)


def local(
    inputs, out_cotangent, skip_cotangent, convolution_weight, convolution_bias, output_weight
):
    start_row = inputs[0]
    output_cotangent_rows = out_cotangent[0]
    skip_cotangent_rows = skip_cotangent[0]
    rows, channels = start_row.shape
    half = rows // 2
    tail = from_behind(start_row[rows - half :], SEQ_AXES, 1)
    earlier1 = jnp.concatenate([tail, start_row[: rows - half]], axis=0)
    first_joined, first_tanh, first_sigmoid, first_hidden = layer_forward_step(
        earlier1, start_row, convolution_weight[0], convolution_bias[0]
    )
    second_layer = start_row + matmul(first_hidden, output_weight[0][:, :channels])
    earlier2 = from_behind(second_layer, SEQ_AXES, 1)
    second_joined, second_tanh, second_sigmoid, second_hidden = layer_forward_step(
        earlier2, second_layer, convolution_weight[1], convolution_bias[1]
    )
    past2, local2, second_conv_output, second_output, second_bias = layer_backward_step(
        second_joined,
        second_tanh,
        second_sigmoid,
        second_hidden,
        convolution_weight[1],
        output_weight[1],
        output_cotangent_rows,
        skip_cotangent_rows,
    )
    carried_state = output_cotangent_rows + local2 + from_behind(past2, SEQ_AXES, -1)
    past1, local1, first_conv_output, first_output, first_bias = layer_backward_step(
        first_joined,
        first_tanh,
        first_sigmoid,
        first_hidden,
        convolution_weight[0],
        output_weight[0],
        carried_state,
        skip_cotangent_rows,
    )
    rim_rows = from_behind(past1[:half], SEQ_AXES, -1)
    input_grad = carried_state + local1 + jnp.concatenate([past1[half:], rim_rows], axis=0)
    devices = lax.axis_size(SEQ_AXES + DP_AXES)
    factor = 1.0 / math.sqrt(rows * devices)
    conv_terms = jnp.concatenate([first_conv_output, second_conv_output], axis=0)
    out_terms = jnp.concatenate([first_output, second_output], axis=0)
    bias_terms = jnp.concatenate([first_bias, second_bias], axis=0)
    bias_cols = bias_terms.reshape(conv_terms.shape[0], -1)
    bias_cols = jnp.pad(bias_cols, ((0, 0), (0, 128 - bias_cols.shape[1])))
    packed = jnp.concatenate([conv_terms, out_terms, bias_cols], axis=1)
    summed = reduce_to_owner(packed) * factor
    conv_width, out_width = conv_terms.shape[1], out_terms.shape[1]
    conv_grad = summed[:, :conv_width]
    out_grad = summed[:, conv_width : conv_width + out_width]
    bias_grad = summed[:, conv_width + out_width : conv_width + out_width + bias_terms.shape[0] // conv_terms.shape[0]]
    bias_grad = bias_grad.reshape(-1)
    return (input_grad[None], conv_grad, out_grad, bias_grad)


def solution(mesh):
    fine = jax.sharding.Mesh(mesh.devices.reshape(4, 2, 8, 2, 2), ("y", "xl", "z", "xh", "c"))
    rows_spec = P(("xh", "c"), ("y", "xl", "z"), None)
    owner = ("y", "xl", "z", "xh", "c")
    return jax.shard_map(
        local,
        mesh=fine,
        in_specs=(rows_spec, rows_spec, rows_spec, P(), P(), P()),
        out_specs=(rows_spec, P(owner, None), P(owner, None), P(owner)),
        check_vma=False,
    )
```

```python
import math

import jax
import jax.numpy as jnp
from jax import lax
from jax.sharding import PartitionSpec as P


SEQ_AXES = ("y", "xl", "z")
DP_AXES = ("xh", "c")


def reduce_rows(block, axis):
    parts = lax.axis_size(axis)
    block = block.reshape(parts, block.shape[0] // parts, block.shape[1])
    return lax.all_to_all(block, axis, 0, 0, tiled=True).sum(axis=0)


def reduce_to_owner(packed):
    rows, width = packed.shape
    halves = lax.all_to_all(packed.reshape(rows, 2, width // 2), "c", 1, 1, tiled=True)
    block = halves.sum(axis=1)
    for axis in ("y", "xl", "z", "xh"):
        block = reduce_rows(block, axis)
    return lax.all_to_all(block, "c", 0, 1, tiled=True)


def from_behind(block, axis, distance):
    devices = range(lax.axis_size(axis))
    route = [(i - distance, i) for i in devices if i - distance in devices]
    return lax.ppermute(block, axis, route)


def matmul(left, right):
    return jnp.dot(left, right, precision=lax.Precision.HIGH, preferred_element_type=jnp.float32)


def contract(left, right, left_dim, right_dim):
    return lax.dot_general(
        left,
        right,
        (((left_dim,), (right_dim,)), ((), ())),
        precision=lax.Precision.HIGH,
        preferred_element_type=jnp.float32,
    )


def layer_forward_step(earlier, values, weight, bias):
    joined = jnp.concatenate([earlier, values], axis=1)
    mixed = matmul(joined, weight) + bias
    width = weight.shape[1] // 2
    tanh_part = jnp.tanh(mixed[:, :width])
    sigm_part = jax.nn.sigmoid(mixed[:, width:])
    return (joined, tanh_part, sigm_part, tanh_part * sigm_part)


def layer_backward_step(
    joined, tanh_part, sigm_part, hidden, weight, out_w, carried_state, skip_cotangent_rows
):
    channels = carried_state.shape[1]
    outer = jnp.concatenate([carried_state, skip_cotangent_rows], axis=1)
    dhidden = contract(outer, out_w, 1, 1)
    dfilter = dhidden * sigm_part * (1.0 - tanh_part * tanh_part)
    dgate = dhidden * tanh_part * sigm_part * (1.0 - sigm_part)
    dmixed = jnp.concatenate([dfilter, dgate], axis=1)
    out_t = contract(outer, hidden, 0, 0)
    conv_g = contract(joined, dmixed, 0, 0)
    bias_g = jnp.sum(dmixed, axis=0)
    back = contract(dmixed, weight, 1, 1)
    return (back[:, :channels], back[:, channels:], conv_g, out_t, bias_g)


def local(
    inputs, out_cotangent, skip_cotangent, convolution_weight, convolution_bias, output_weight
):
    start_row = inputs[0]
    output_cotangent_rows = out_cotangent[0]
    skip_cotangent_rows = skip_cotangent[0]
    rows, channels = start_row.shape
    half = rows // 2
    tail = from_behind(start_row[rows - half :], SEQ_AXES, 1)
    earlier1 = jnp.concatenate([tail, start_row[: rows - half]], axis=0)
    first_joined, first_tanh, first_sigmoid, first_hidden = layer_forward_step(
        earlier1, start_row, convolution_weight[0], convolution_bias[0]
    )
    second_layer = start_row + matmul(first_hidden, output_weight[0][:, :channels])
    earlier2 = from_behind(second_layer, SEQ_AXES, 1)
    second_joined, second_tanh, second_sigmoid, second_hidden = layer_forward_step(
        earlier2, second_layer, convolution_weight[1], convolution_bias[1]
    )
    past2, local2, second_conv_output, second_output, second_bias = layer_backward_step(
        second_joined,
        second_tanh,
        second_sigmoid,
        second_hidden,
        convolution_weight[1],
        output_weight[1],
        output_cotangent_rows,
        skip_cotangent_rows,
    )
    carried_state = output_cotangent_rows + local2 + from_behind(past2, SEQ_AXES, -1)
    past1, local1, first_conv_output, first_output, first_bias = layer_backward_step(
        first_joined,
        first_tanh,
        first_sigmoid,
        first_hidden,
        convolution_weight[0],
        output_weight[0],
        carried_state,
        skip_cotangent_rows,
    )
    rim_rows = from_behind(past1[:half], SEQ_AXES, -1)
    input_grad = carried_state + local1 + jnp.concatenate([past1[half:], rim_rows], axis=0)
    devices = lax.axis_size(SEQ_AXES + DP_AXES)
    factor = 1.0 / math.sqrt(rows * devices)
    conv_terms = jnp.concatenate([first_conv_output, second_conv_output], axis=0)
    out_terms = jnp.concatenate([first_output, second_output], axis=0)
    bias_terms = jnp.concatenate([first_bias, second_bias], axis=0)
    bias_cols = bias_terms.reshape(conv_terms.shape[0], -1)
    bias_cols = jnp.pad(bias_cols, ((0, 0), (0, 128 - bias_cols.shape[1])))
    packed = jnp.concatenate([conv_terms, out_terms, bias_cols], axis=1)
    summed = reduce_to_owner(packed) * factor
    conv_width, out_width = conv_terms.shape[1], out_terms.shape[1]
    conv_grad = summed[:, :conv_width]
    out_grad = summed[:, conv_width : conv_width + out_width]
    bias_grad = summed[:, conv_width + out_width : conv_width + out_width + bias_terms.shape[0] // conv_terms.shape[0]]
    bias_grad = bias_grad.reshape(-1)
    return (input_grad[None], conv_grad, out_grad, bias_grad)


def solution(mesh):
    fine = jax.sharding.Mesh(mesh.devices.reshape(4, 2, 8, 2, 2), ("y", "xl", "z", "xh", "c"))
    rows_spec = P(("xh", "c"), ("y", "xl", "z"), None)
    owner = ("y", "xl", "z", "xh", "c")
    return jax.shard_map(
        local,
        mesh=fine,
        in_specs=(rows_spec, rows_spec, rows_spec, P(), P(), P()),
        out_specs=(rows_spec, P(owner, None), P(owner, None), P(owner)),
        check_vma=False,
    )
```

```python
import math

import jax
import jax.numpy as jnp
from jax import lax
from jax.sharding import PartitionSpec as P


SEQ_AXES = ("y", "xl", "z")
DP_AXES = ("xh", "c")


def reduce_rows(block, axis):
    parts = lax.axis_size(axis)
    block = block.reshape(parts, block.shape[0] // parts, block.shape[1])
    return lax.all_to_all(block, axis, 0, 0, tiled=True).sum(axis=0)


def reduce_to_owner(packed):
    rows, width = packed.shape
    sizes = [lax.axis_size(a) for a in ("y", "xl", "z", "xh", "c")]
    block = packed.reshape(*sizes, -1, width).transpose(4, 3, 1, 0, 2, 5, 6).reshape(rows, width)
    for axis in ("c", ("xh", "xl"), "y", "z"):
        block = reduce_rows(block, axis)
    return block


def from_behind(block, axis, distance):
    devices = range(lax.axis_size(axis))
    route = [(i - distance, i) for i in devices if i - distance in devices]
    return lax.ppermute(block, axis, route)


def matmul(left, right):
    return jnp.dot(left, right, precision=lax.Precision.HIGH, preferred_element_type=jnp.float32)


def contract(left, right, left_dim, right_dim):
    return lax.dot_general(
        left,
        right,
        (((left_dim,), (right_dim,)), ((), ())),
        precision=lax.Precision.HIGH,
        preferred_element_type=jnp.float32,
    )


def layer_forward_step(earlier, values, weight, bias):
    joined = jnp.concatenate([earlier, values], axis=1)
    mixed = matmul(joined, weight) + bias
    width = weight.shape[1] // 2
    tanh_part = jnp.tanh(mixed[:, :width])
    sigm_part = jax.nn.sigmoid(mixed[:, width:])
    return (joined, tanh_part, sigm_part, tanh_part * sigm_part)


def layer_backward_step(
    joined, tanh_part, sigm_part, hidden, weight, out_w, carried_state, skip_cotangent_rows
):
    channels = carried_state.shape[1]
    outer = jnp.concatenate([carried_state, skip_cotangent_rows], axis=1)
    dhidden = contract(outer, out_w, 1, 1)
    dfilter = dhidden * sigm_part * (1.0 - tanh_part * tanh_part)
    dgate = dhidden * tanh_part * sigm_part * (1.0 - sigm_part)
    dmixed = jnp.concatenate([dfilter, dgate], axis=1)
    out_t = contract(outer, hidden, 0, 0)
    conv_g = contract(joined, dmixed, 0, 0)
    bias_g = jnp.sum(dmixed, axis=0)
    back = contract(dmixed, weight, 1, 1)
    return (back[:, :channels], back[:, channels:], conv_g, out_t, bias_g)


def local(
    inputs, out_cotangent, skip_cotangent, convolution_weight, convolution_bias, output_weight
):
    start_row = inputs[0]
    output_cotangent_rows = out_cotangent[0]
    skip_cotangent_rows = skip_cotangent[0]
    rows, channels = start_row.shape
    half = rows // 2
    tail = from_behind(start_row[rows - half :], SEQ_AXES, 1)
    earlier1 = jnp.concatenate([tail, start_row[: rows - half]], axis=0)
    first_joined, first_tanh, first_sigmoid, first_hidden = layer_forward_step(
        earlier1, start_row, convolution_weight[0], convolution_bias[0]
    )
    second_layer = start_row + matmul(first_hidden, output_weight[0][:, :channels])
    earlier2 = from_behind(second_layer, SEQ_AXES, 1)
    second_joined, second_tanh, second_sigmoid, second_hidden = layer_forward_step(
        earlier2, second_layer, convolution_weight[1], convolution_bias[1]
    )
    past2, local2, second_conv_output, second_output, second_bias = layer_backward_step(
        second_joined,
        second_tanh,
        second_sigmoid,
        second_hidden,
        convolution_weight[1],
        output_weight[1],
        output_cotangent_rows,
        skip_cotangent_rows,
    )
    carried_state = output_cotangent_rows + local2 + from_behind(past2, SEQ_AXES, -1)
    past1, local1, first_conv_output, first_output, first_bias = layer_backward_step(
        first_joined,
        first_tanh,
        first_sigmoid,
        first_hidden,
        convolution_weight[0],
        output_weight[0],
        carried_state,
        skip_cotangent_rows,
    )
    rim_rows = from_behind(past1[:half], SEQ_AXES, -1)
    input_grad = carried_state + local1 + jnp.concatenate([past1[half:], rim_rows], axis=0)
    devices = lax.axis_size(SEQ_AXES + DP_AXES)
    factor = 1.0 / math.sqrt(rows * devices)
    conv_terms = jnp.concatenate([first_conv_output, second_conv_output], axis=0)
    out_terms = jnp.concatenate([first_output, second_output], axis=0)
    bias_terms = jnp.concatenate([first_bias, second_bias], axis=0)
    bias_cols = bias_terms.reshape(conv_terms.shape[0], -1)
    bias_cols = jnp.pad(bias_cols, ((0, 0), (0, 128 - bias_cols.shape[1])))
    packed = jnp.concatenate([conv_terms, out_terms, bias_cols], axis=1)
    summed = reduce_to_owner(packed) * factor
    conv_width, out_width = conv_terms.shape[1], out_terms.shape[1]
    conv_grad = summed[:, :conv_width]
    out_grad = summed[:, conv_width : conv_width + out_width]
    bias_grad = summed[:, conv_width + out_width : conv_width + out_width + bias_terms.shape[0] // conv_terms.shape[0]]
    bias_grad = bias_grad.reshape(-1)
    return (input_grad[None], conv_grad, out_grad, bias_grad)


def solution(mesh):
    fine = jax.sharding.Mesh(mesh.devices.reshape(4, 2, 8, 2, 2), ("y", "xl", "z", "xh", "c"))
    rows_spec = P(("xh", "c"), ("y", "xl", "z"), None)
    owner = ("y", "xl", "z", "xh", "c")
    return jax.shard_map(
        local,
        mesh=fine,
        in_specs=(rows_spec, rows_spec, rows_spec, P(), P(), P()),
        out_specs=(rows_spec, P(owner, None), P(owner, None), P(owner)),
        check_vma=False,
    )
```

```python
import math

import jax
import jax.numpy as jnp
from jax import lax
from jax.sharding import PartitionSpec as P


SEQ_AXES = ("y", "xl", "z")
DP_AXES = ("xh", "c")


def reduce_rows(block, axis):
    parts = lax.axis_size(axis)
    block = block.reshape(parts, block.shape[0] // parts, block.shape[1])
    return lax.all_to_all(block, axis, 0, 0, tiled=True).sum(axis=0)


def reduce_to_owner(packed):
    rows, width = packed.shape
    y, xl, z, xh, c = [lax.axis_size(a) for a in ("y", "xl", "z", "xh", "c")]
    block = packed.reshape(y, xl, z, xh, -1, width).transpose(3, 1, 0, 2, 4, 5).reshape(rows, width)
    halves = lax.all_to_all(block.reshape(rows, c, width // c), "c", 1, 1, tiled=True)
    block = halves.sum(axis=1)
    for axis in (("xh", "xl"), "y", "z"):
        block = reduce_rows(block, axis)
    return lax.all_to_all(block, "c", 0, 1, tiled=True)


def from_behind(block, axis, distance):
    devices = range(lax.axis_size(axis))
    route = [(i - distance, i) for i in devices if i - distance in devices]
    return lax.ppermute(block, axis, route)


def matmul(left, right):
    return jnp.dot(left, right, precision=lax.Precision.HIGH, preferred_element_type=jnp.float32)


def contract(left, right, left_dim, right_dim):
    return lax.dot_general(
        left,
        right,
        (((left_dim,), (right_dim,)), ((), ())),
        precision=lax.Precision.HIGH,
        preferred_element_type=jnp.float32,
    )


def layer_forward_step(earlier, values, weight, bias):
    joined = jnp.concatenate([earlier, values], axis=1)
    mixed = matmul(joined, weight) + bias
    width = weight.shape[1] // 2
    tanh_part = jnp.tanh(mixed[:, :width])
    sigm_part = jax.nn.sigmoid(mixed[:, width:])
    return (joined, tanh_part, sigm_part, tanh_part * sigm_part)


def layer_backward_step(
    joined, tanh_part, sigm_part, hidden, weight, out_w, carried_state, skip_cotangent_rows
):
    channels = carried_state.shape[1]
    outer = jnp.concatenate([carried_state, skip_cotangent_rows], axis=1)
    dhidden = contract(outer, out_w, 1, 1)
    dfilter = dhidden * sigm_part * (1.0 - tanh_part * tanh_part)
    dgate = dhidden * tanh_part * sigm_part * (1.0 - sigm_part)
    dmixed = jnp.concatenate([dfilter, dgate], axis=1)
    out_t = contract(outer, hidden, 0, 0)
    conv_g = contract(joined, dmixed, 0, 0)
    bias_g = jnp.sum(dmixed, axis=0)
    back = contract(dmixed, weight, 1, 1)
    return (back[:, :channels], back[:, channels:], conv_g, out_t, bias_g)


def local(
    inputs, out_cotangent, skip_cotangent, convolution_weight, convolution_bias, output_weight
):
    start_row = inputs[0]
    output_cotangent_rows = out_cotangent[0]
    skip_cotangent_rows = skip_cotangent[0]
    rows, channels = start_row.shape
    half = rows // 2
    tail = from_behind(start_row[rows - half :], SEQ_AXES, 1)
    earlier1 = jnp.concatenate([tail, start_row[: rows - half]], axis=0)
    first_joined, first_tanh, first_sigmoid, first_hidden = layer_forward_step(
        earlier1, start_row, convolution_weight[0], convolution_bias[0]
    )
    second_layer = start_row + matmul(first_hidden, output_weight[0][:, :channels])
    earlier2 = from_behind(second_layer, SEQ_AXES, 1)
    second_joined, second_tanh, second_sigmoid, second_hidden = layer_forward_step(
        earlier2, second_layer, convolution_weight[1], convolution_bias[1]
    )
    past2, local2, second_conv_output, second_output, second_bias = layer_backward_step(
        second_joined,
        second_tanh,
        second_sigmoid,
        second_hidden,
        convolution_weight[1],
        output_weight[1],
        output_cotangent_rows,
        skip_cotangent_rows,
    )
    carried_state = output_cotangent_rows + local2 + from_behind(past2, SEQ_AXES, -1)
    past1, local1, first_conv_output, first_output, first_bias = layer_backward_step(
        first_joined,
        first_tanh,
        first_sigmoid,
        first_hidden,
        convolution_weight[0],
        output_weight[0],
        carried_state,
        skip_cotangent_rows,
    )
    rim_rows = from_behind(past1[:half], SEQ_AXES, -1)
    input_grad = carried_state + local1 + jnp.concatenate([past1[half:], rim_rows], axis=0)
    devices = lax.axis_size(SEQ_AXES + DP_AXES)
    factor = 1.0 / math.sqrt(rows * devices)
    conv_terms = jnp.concatenate([first_conv_output, second_conv_output], axis=0)
    out_terms = jnp.concatenate([first_output, second_output], axis=0)
    bias_terms = jnp.concatenate([first_bias, second_bias], axis=0)
    bias_cols = bias_terms.reshape(conv_terms.shape[0], -1)
    bias_cols = jnp.pad(bias_cols, ((0, 0), (0, 128 - bias_cols.shape[1])))
    packed = jnp.concatenate([conv_terms, out_terms, bias_cols], axis=1)
    summed = reduce_to_owner(packed) * factor
    conv_width, out_width = conv_terms.shape[1], out_terms.shape[1]
    conv_grad = summed[:, :conv_width]
    out_grad = summed[:, conv_width : conv_width + out_width]
    bias_grad = summed[:, conv_width + out_width : conv_width + out_width + bias_terms.shape[0] // conv_terms.shape[0]]
    bias_grad = bias_grad.reshape(-1)
    return (input_grad[None], conv_grad, out_grad, bias_grad)


def solution(mesh):
    fine = jax.sharding.Mesh(mesh.devices.reshape(4, 2, 8, 2, 2), ("y", "xl", "z", "xh", "c"))
    rows_spec = P(("xh", "c"), ("y", "xl", "z"), None)
    owner = ("y", "xl", "z", "xh", "c")
    return jax.shard_map(
        local,
        mesh=fine,
        in_specs=(rows_spec, rows_spec, rows_spec, P(), P(), P()),
        out_specs=(rows_spec, P(owner, None), P(owner, None), P(owner)),
        check_vma=False,
    )
```

```python
import math

import jax
import jax.numpy as jnp
from jax import lax
from jax.sharding import PartitionSpec as P


SEQ_AXES = ("y", "xl", "z")
DP_AXES = ("xh", "c")


def reduce_rows(block, axis):
    parts = lax.axis_size(axis)
    block = block.reshape(parts, block.shape[0] // parts, block.shape[1])
    return lax.all_to_all(block, axis, 0, 0, tiled=True).sum(axis=0)


def reduce_to_owner(packed):
    rows, width = packed.shape
    sizes = [lax.axis_size(a) for a in ("y", "xl", "z", "xh", "c")]
    block = packed.reshape(*sizes, -1, width).transpose(4, 3, 1, 0, 2, 5, 6).reshape(rows, width)
    for axis in ("c", ("xh", "xl"), "y", "z"):
        block = reduce_rows(block, axis)
    return block


def from_behind(block, axis, distance):
    devices = range(lax.axis_size(axis))
    route = [(i - distance, i) for i in devices if i - distance in devices]
    return lax.ppermute(block, axis, route)


def matmul(left, right):
    return jnp.dot(left, right, precision=lax.Precision.HIGH, preferred_element_type=jnp.float32)


def contract(left, right, left_dim, right_dim):
    return lax.dot_general(
        left,
        right,
        (((left_dim,), (right_dim,)), ((), ())),
        precision=lax.Precision.HIGH,
        preferred_element_type=jnp.float32,
    )


def layer_forward_step(earlier, values, weight, bias):
    joined = jnp.concatenate([earlier, values], axis=1)
    taps = earlier.shape[1]
    mixed = matmul(values, weight[taps:]) + matmul(earlier, weight[:taps]) + bias
    width = weight.shape[1] // 2
    tanh_part = jnp.tanh(mixed[:, :width])
    sigm_part = jax.nn.sigmoid(mixed[:, width:])
    return (joined, tanh_part, sigm_part, tanh_part * sigm_part)


def layer_backward_step(
    joined, tanh_part, sigm_part, hidden, weight, out_w, carried_state, skip_cotangent_rows
):
    channels = carried_state.shape[1]
    outer = jnp.concatenate([carried_state, skip_cotangent_rows], axis=1)
    dhidden = contract(skip_cotangent_rows, out_w[:, channels:], 1, 1)
    dhidden = dhidden + contract(carried_state, out_w[:, :channels], 1, 1)
    dfilter = dhidden * sigm_part * (1.0 - tanh_part * tanh_part)
    dgate = dhidden * tanh_part * sigm_part * (1.0 - sigm_part)
    dmixed = jnp.concatenate([dfilter, dgate], axis=1)
    out_t = contract(outer, hidden, 0, 0)
    conv_g = contract(joined, dmixed, 0, 0)
    bias_g = jnp.sum(dmixed, axis=0)
    back = contract(dmixed, weight, 1, 1)
    return (back[:, :channels], back[:, channels:], conv_g, out_t, bias_g)


def local(
    inputs, out_cotangent, skip_cotangent, convolution_weight, convolution_bias, output_weight
):
    start_row = inputs[0]
    output_cotangent_rows = out_cotangent[0]
    skip_cotangent_rows = skip_cotangent[0]
    rows, channels = start_row.shape
    half = rows // 2
    tail = from_behind(start_row[rows - half :], SEQ_AXES, 1)
    earlier1 = jnp.concatenate([tail, start_row[: rows - half]], axis=0)
    first_joined, first_tanh, first_sigmoid, first_hidden = layer_forward_step(
        earlier1, start_row, convolution_weight[0], convolution_bias[0]
    )
    second_layer = start_row + matmul(first_hidden, output_weight[0][:, :channels])
    earlier2 = from_behind(second_layer, SEQ_AXES, 1)
    second_joined, second_tanh, second_sigmoid, second_hidden = layer_forward_step(
        earlier2, second_layer, convolution_weight[1], convolution_bias[1]
    )
    past2, local2, second_conv_output, second_output, second_bias = layer_backward_step(
        second_joined,
        second_tanh,
        second_sigmoid,
        second_hidden,
        convolution_weight[1],
        output_weight[1],
        output_cotangent_rows,
        skip_cotangent_rows,
    )
    carried_state = output_cotangent_rows + local2 + from_behind(past2, SEQ_AXES, -1)
    past1, local1, first_conv_output, first_output, first_bias = layer_backward_step(
        first_joined,
        first_tanh,
        first_sigmoid,
        first_hidden,
        convolution_weight[0],
        output_weight[0],
        carried_state,
        skip_cotangent_rows,
    )
    rim_rows = from_behind(past1[:half], SEQ_AXES, -1)
    input_grad = carried_state + local1 + jnp.concatenate([past1[half:], rim_rows], axis=0)
    devices = lax.axis_size(SEQ_AXES + DP_AXES)
    factor = 1.0 / math.sqrt(rows * devices)
    conv_terms = jnp.concatenate([first_conv_output, second_conv_output], axis=0)
    out_terms = jnp.concatenate([first_output, second_output], axis=0)
    bias_terms = jnp.concatenate([first_bias, second_bias], axis=0)
    bias_cols = bias_terms.reshape(conv_terms.shape[0], -1)
    bias_cols = jnp.pad(bias_cols, ((0, 0), (0, 128 - bias_cols.shape[1])))
    packed = jnp.concatenate([conv_terms, out_terms, bias_cols], axis=1)
    summed = reduce_to_owner(packed) * factor
    conv_width, out_width = conv_terms.shape[1], out_terms.shape[1]
    conv_grad = summed[:, :conv_width]
    out_grad = summed[:, conv_width : conv_width + out_width]
    bias_grad = summed[:, conv_width + out_width : conv_width + out_width + bias_terms.shape[0] // conv_terms.shape[0]]
    bias_grad = bias_grad.reshape(-1)
    return (input_grad[None], conv_grad, out_grad, bias_grad)


def solution(mesh):
    fine = jax.sharding.Mesh(mesh.devices.reshape(4, 2, 8, 2, 2), ("y", "xl", "z", "xh", "c"))
    rows_spec = P(("xh", "c"), ("y", "xl", "z"), None)
    owner = ("y", "xl", "z", "xh", "c")
    return jax.shard_map(
        local,
        mesh=fine,
        in_specs=(rows_spec, rows_spec, rows_spec, P(), P(), P()),
        out_specs=(rows_spec, P(owner, None), P(owner, None), P(owner)),
        check_vma=False,
    )
```

```python
import math

import jax
import jax.numpy as jnp
from jax import lax
from jax.sharding import PartitionSpec as P


SEQ_AXES = ("y", "xl", "z")
DP_AXES = ("xh", "c")


def reduce_rows(block, axis):
    parts = lax.axis_size(axis)
    block = block.reshape(parts, block.shape[0] // parts, block.shape[1])
    return lax.all_to_all(block, axis, 0, 0, tiled=True).sum(axis=0)


def reduce_to_owner(packed):
    for axis in ("c", ("xh", "xl"), "y", "z"):
        packed = reduce_rows(packed, axis)
    return packed


def owner_order(block):
    sizes = [lax.axis_size(a) for a in ("xl", "z", "xh", "c")]
    rows, channels = block.shape
    block = block.reshape(rows, 2, *sizes, -1).transpose(0, 5, 4, 2, 1, 3, 6)
    return block.reshape(rows, channels)


def from_behind(block, axis, distance):
    devices = range(lax.axis_size(axis))
    route = [(i - distance, i) for i in devices if i - distance in devices]
    return lax.ppermute(block, axis, route)


def matmul(left, right):
    return jnp.dot(left, right, precision=lax.Precision.HIGH, preferred_element_type=jnp.float32)


def contract(left, right, left_dim, right_dim):
    return lax.dot_general(
        left,
        right,
        (((left_dim,), (right_dim,)), ((), ())),
        precision=lax.Precision.HIGH,
        preferred_element_type=jnp.float32,
    )


def layer_forward_step(earlier, values, weight, bias):
    joined = jnp.concatenate([earlier, values], axis=1)
    taps = earlier.shape[1]
    mixed = matmul(values, weight[taps:]) + matmul(earlier, weight[:taps]) + bias
    width = weight.shape[1] // 2
    tanh_part = jnp.tanh(mixed[:, :width])
    sigm_part = jax.nn.sigmoid(mixed[:, width:])
    return (joined, tanh_part, sigm_part, tanh_part * sigm_part)


def layer_backward_step(
    joined, tanh_part, sigm_part, hidden, weight, out_w, carried_state, skip_cotangent_rows
):
    channels = carried_state.shape[1]
    outer = jnp.concatenate([carried_state, skip_cotangent_rows], axis=1)
    dhidden = contract(skip_cotangent_rows, out_w[:, channels:], 1, 1)
    dhidden = dhidden + contract(carried_state, out_w[:, :channels], 1, 1)
    dfilter = dhidden * sigm_part * (1.0 - tanh_part * tanh_part)
    dgate = dhidden * tanh_part * sigm_part * (1.0 - sigm_part)
    dmixed = jnp.concatenate([dfilter, dgate], axis=1)
    out_t = contract(owner_order(outer), hidden, 0, 0)
    conv_g = contract(owner_order(joined), dmixed, 0, 0)
    bias_g = jnp.sum(dmixed, axis=0)
    back = contract(dmixed, weight, 1, 1)
    return (back[:, :channels], back[:, channels:], conv_g, out_t, bias_g)


def local(
    inputs, out_cotangent, skip_cotangent, convolution_weight, convolution_bias, output_weight
):
    start_row = inputs[0]
    output_cotangent_rows = out_cotangent[0]
    skip_cotangent_rows = skip_cotangent[0]
    rows, channels = start_row.shape
    half = rows // 2
    tail = from_behind(start_row[rows - half :], SEQ_AXES, 1)
    earlier1 = jnp.concatenate([tail, start_row[: rows - half]], axis=0)
    first_joined, first_tanh, first_sigmoid, first_hidden = layer_forward_step(
        earlier1, start_row, convolution_weight[0], convolution_bias[0]
    )
    second_layer = start_row + matmul(first_hidden, output_weight[0][:, :channels])
    earlier2 = from_behind(second_layer, SEQ_AXES, 1)
    second_joined, second_tanh, second_sigmoid, second_hidden = layer_forward_step(
        earlier2, second_layer, convolution_weight[1], convolution_bias[1]
    )
    past2, local2, second_conv_output, second_output, second_bias = layer_backward_step(
        second_joined,
        second_tanh,
        second_sigmoid,
        second_hidden,
        convolution_weight[1],
        output_weight[1],
        output_cotangent_rows,
        skip_cotangent_rows,
    )
    carried_state = output_cotangent_rows + local2 + from_behind(past2, SEQ_AXES, -1)
    past1, local1, first_conv_output, first_output, first_bias = layer_backward_step(
        first_joined,
        first_tanh,
        first_sigmoid,
        first_hidden,
        convolution_weight[0],
        output_weight[0],
        carried_state,
        skip_cotangent_rows,
    )
    rim_rows = from_behind(past1[:half], SEQ_AXES, -1)
    input_grad = carried_state + local1 + jnp.concatenate([past1[half:], rim_rows], axis=0)
    devices = lax.axis_size(SEQ_AXES + DP_AXES)
    factor = 1.0 / math.sqrt(rows * devices)
    groups = lax.axis_size(("c", "xh", "xl"))

    def interleave(first, second):
        both = jnp.stack([first.reshape(groups, -1, first.shape[1]), second.reshape(groups, -1, second.shape[1])], axis=1)
        return both.reshape(-1, first.shape[1])

    conv_terms = interleave(first_conv_output, second_conv_output)
    out_terms = interleave(first_output, second_output)
    bias_terms = jnp.concatenate([first_bias, second_bias], axis=0)
    bias_per_row = bias_terms.shape[0] // conv_terms.shape[0]
    sizes = [lax.axis_size(a) for a in ("y", "xl", "z", "xh", "c")]
    bias_terms = bias_terms.reshape(*sizes, -1).transpose(4, 3, 1, 0, 2, 5)
    bias_cols = bias_terms.reshape(conv_terms.shape[0], -1)
    bias_cols = jnp.pad(bias_cols, ((0, 0), (0, 128 - bias_cols.shape[1])))
    packed = jnp.concatenate([conv_terms, out_terms, bias_cols], axis=1)
    summed = reduce_to_owner(packed) * factor
    conv_width, out_width = conv_terms.shape[1], out_terms.shape[1]
    conv_grad = summed[:, :conv_width]
    out_grad = summed[:, conv_width : conv_width + out_width]
    bias_grad = summed[:, conv_width + out_width : conv_width + out_width + bias_per_row]
    bias_grad = bias_grad.reshape(-1)
    return (input_grad[None], conv_grad, out_grad, bias_grad)


def solution(mesh):
    fine = jax.sharding.Mesh(mesh.devices.reshape(4, 2, 8, 2, 2), ("y", "xl", "z", "xh", "c"))
    rows_spec = P(("xh", "c"), ("y", "xl", "z"), None)
    owner = ("y", "xl", "z", "xh", "c")
    return jax.shard_map(
        local,
        mesh=fine,
        in_specs=(rows_spec, rows_spec, rows_spec, P(), P(), P()),
        out_specs=(rows_spec, P(owner, None), P(owner, None), P(owner)),
        check_vma=False,
    )
```

```python
import math

import jax
import jax.numpy as jnp
from jax import lax
from jax.sharding import PartitionSpec as P


SEQ_AXES = ("y", "xl", "z")
DP_AXES = ("xh", "c")


def reduce_rows(block, axis):
    parts = lax.axis_size(axis)
    block = block.reshape(parts, block.shape[0] // parts, block.shape[1])
    return lax.all_to_all(block, axis, 0, 0, tiled=True).sum(axis=0)


def reduce_to_owner(packed):
    rows, width = packed.shape
    sizes = [lax.axis_size(a) for a in ("y", "xl", "z", "xh", "c")]
    block = packed.reshape(*sizes, -1, width).transpose(4, 1, 3, 0, 2, 5, 6).reshape(rows, width)
    for axis in ("c", "xl", "xh", "y", "z"):
        block = reduce_rows(block, axis)
    return block


def from_behind(block, axis, distance):
    devices = range(lax.axis_size(axis))
    route = [(i - distance, i) for i in devices if i - distance in devices]
    return lax.ppermute(block, axis, route)


def matmul(left, right):
    return jnp.dot(left, right, precision=lax.Precision.HIGH, preferred_element_type=jnp.float32)


def contract(left, right, left_dim, right_dim):
    return lax.dot_general(
        left,
        right,
        (((left_dim,), (right_dim,)), ((), ())),
        precision=lax.Precision.HIGH,
        preferred_element_type=jnp.float32,
    )


def layer_forward_step(earlier, values, weight, bias):
    joined = jnp.concatenate([earlier, values], axis=1)
    taps = earlier.shape[1]
    mixed = matmul(values, weight[taps:]) + matmul(earlier, weight[:taps]) + bias
    width = weight.shape[1] // 2
    tanh_part = jnp.tanh(mixed[:, :width])
    sigm_part = jax.nn.sigmoid(mixed[:, width:])
    return (joined, tanh_part, sigm_part, tanh_part * sigm_part)


def layer_backward_step(
    joined, tanh_part, sigm_part, hidden, weight, out_w, carried_state, skip_cotangent_rows
):
    channels = carried_state.shape[1]
    outer = jnp.concatenate([carried_state, skip_cotangent_rows], axis=1)
    dhidden = contract(skip_cotangent_rows, out_w[:, channels:], 1, 1)
    dhidden = dhidden + contract(carried_state, out_w[:, :channels], 1, 1)
    dfilter = dhidden * sigm_part * (1.0 - tanh_part * tanh_part)
    dgate = dhidden * tanh_part * sigm_part * (1.0 - sigm_part)
    dmixed = jnp.concatenate([dfilter, dgate], axis=1)
    out_t = contract(outer, hidden, 0, 0)
    conv_g = contract(joined, dmixed, 0, 0)
    bias_g = jnp.sum(dmixed, axis=0)
    back = contract(dmixed, weight, 1, 1)
    return (back[:, :channels], back[:, channels:], conv_g, out_t, bias_g)


def local(
    inputs, out_cotangent, skip_cotangent, convolution_weight, convolution_bias, output_weight
):
    start_row = inputs[0]
    output_cotangent_rows = out_cotangent[0]
    skip_cotangent_rows = skip_cotangent[0]
    rows, channels = start_row.shape
    half = rows // 2
    tail = from_behind(start_row[rows - half :], SEQ_AXES, 1)
    earlier1 = jnp.concatenate([tail, start_row[: rows - half]], axis=0)
    first_joined, first_tanh, first_sigmoid, first_hidden = layer_forward_step(
        earlier1, start_row, convolution_weight[0], convolution_bias[0]
    )
    second_layer = start_row + matmul(first_hidden, output_weight[0][:, :channels])
    earlier2 = from_behind(second_layer, SEQ_AXES, 1)
    second_joined, second_tanh, second_sigmoid, second_hidden = layer_forward_step(
        earlier2, second_layer, convolution_weight[1], convolution_bias[1]
    )
    past2, local2, second_conv_output, second_output, second_bias = layer_backward_step(
        second_joined,
        second_tanh,
        second_sigmoid,
        second_hidden,
        convolution_weight[1],
        output_weight[1],
        output_cotangent_rows,
        skip_cotangent_rows,
    )
    carried_state = output_cotangent_rows + local2 + from_behind(past2, SEQ_AXES, -1)
    past1, local1, first_conv_output, first_output, first_bias = layer_backward_step(
        first_joined,
        first_tanh,
        first_sigmoid,
        first_hidden,
        convolution_weight[0],
        output_weight[0],
        carried_state,
        skip_cotangent_rows,
    )
    rim_rows = from_behind(past1[:half], SEQ_AXES, -1)
    input_grad = carried_state + local1 + jnp.concatenate([past1[half:], rim_rows], axis=0)
    devices = lax.axis_size(SEQ_AXES + DP_AXES)
    factor = 1.0 / math.sqrt(rows * devices)
    conv_terms = jnp.concatenate([first_conv_output, second_conv_output], axis=0)
    out_terms = jnp.concatenate([first_output, second_output], axis=0)
    bias_terms = jnp.concatenate([first_bias, second_bias], axis=0)
    bias_cols = bias_terms.reshape(conv_terms.shape[0], -1)
    bias_cols = jnp.pad(bias_cols, ((0, 0), (0, 128 - bias_cols.shape[1])))
    packed = jnp.concatenate([conv_terms, out_terms, bias_cols], axis=1)
    summed = reduce_to_owner(packed) * factor
    conv_width, out_width = conv_terms.shape[1], out_terms.shape[1]
    conv_grad = summed[:, :conv_width]
    out_grad = summed[:, conv_width : conv_width + out_width]
    bias_grad = summed[:, conv_width + out_width : conv_width + out_width + bias_terms.shape[0] // conv_terms.shape[0]]
    bias_grad = bias_grad.reshape(-1)
    return (input_grad[None], conv_grad, out_grad, bias_grad)


def solution(mesh):
    fine = jax.sharding.Mesh(mesh.devices.reshape(4, 2, 8, 2, 2), ("y", "xl", "z", "xh", "c"))
    rows_spec = P(("xh", "c"), ("y", "xl", "z"), None)
    owner = ("y", "xl", "z", "xh", "c")
    return jax.shard_map(
        local,
        mesh=fine,
        in_specs=(rows_spec, rows_spec, rows_spec, P(), P(), P()),
        out_specs=(rows_spec, P(owner, None), P(owner, None), P(owner)),
        check_vma=False,
    )
```

```python
import math

import jax
import jax.numpy as jnp
from jax import lax
from jax.sharding import PartitionSpec as P


SEQ_AXES = ("y", "xl", "z")
DP_AXES = ("xh", "c")


def reduce_rows(block, axis):
    parts = lax.axis_size(axis)
    block = block.reshape(parts, block.shape[0] // parts, block.shape[1])
    return lax.all_to_all(block, axis, 0, 0, tiled=True).sum(axis=0)


def owner_rows(terms):
    rows, width = terms.shape
    sizes = [lax.axis_size(a) for a in ("y", "xl", "z", "xh", "c")]
    return terms.reshape(*sizes, -1, width).transpose(4, 3, 1, 0, 2, 5, 6).reshape(rows, width)


def reduce_to_owner(block):
    for axis in ("c", ("xh", "xl"), "y", "z"):
        block = reduce_rows(block, axis)
    return block


def from_behind(block, axis, distance):
    devices = range(lax.axis_size(axis))
    route = [(i - distance, i) for i in devices if i - distance in devices]
    return lax.ppermute(block, axis, route)


def matmul(left, right):
    return jnp.dot(left, right, precision=lax.Precision.HIGH, preferred_element_type=jnp.float32)


def contract(left, right, left_dim, right_dim):
    return lax.dot_general(
        left,
        right,
        (((left_dim,), (right_dim,)), ((), ())),
        precision=lax.Precision.HIGH,
        preferred_element_type=jnp.float32,
    )


def layer_forward_step(earlier, values, weight, bias):
    joined = jnp.concatenate([earlier, values], axis=1)
    taps = earlier.shape[1]
    mixed = matmul(values, weight[taps:]) + matmul(earlier, weight[:taps]) + bias
    width = weight.shape[1] // 2
    tanh_part = jnp.tanh(mixed[:, :width])
    sigm_part = jax.nn.sigmoid(mixed[:, width:])
    return (joined, tanh_part, sigm_part, tanh_part * sigm_part)


def layer_backward_step(
    joined, tanh_part, sigm_part, hidden, weight, out_w, carried_state, skip_cotangent_rows
):
    channels = carried_state.shape[1]
    outer = jnp.concatenate([carried_state, skip_cotangent_rows], axis=1)
    dhidden = contract(skip_cotangent_rows, out_w[:, channels:], 1, 1)
    dhidden = dhidden + contract(carried_state, out_w[:, :channels], 1, 1)
    dfilter = dhidden * sigm_part * (1.0 - tanh_part * tanh_part)
    dgate = dhidden * tanh_part * sigm_part * (1.0 - sigm_part)
    dmixed = jnp.concatenate([dfilter, dgate], axis=1)
    out_t = contract(outer, hidden, 0, 0)
    conv_g = contract(joined, dmixed, 0, 0)
    bias_g = jnp.sum(dmixed, axis=0)
    back = contract(dmixed, weight, 1, 1)
    return (back[:, :channels], back[:, channels:], conv_g, out_t, bias_g)


def local(
    inputs, out_cotangent, skip_cotangent, convolution_weight, convolution_bias, output_weight
):
    start_row = inputs[0]
    output_cotangent_rows = out_cotangent[0]
    skip_cotangent_rows = skip_cotangent[0]
    rows, channels = start_row.shape
    half = rows // 2
    tail = from_behind(start_row[rows - half :], SEQ_AXES, 1)
    earlier1 = jnp.concatenate([tail, start_row[: rows - half]], axis=0)
    first_joined, first_tanh, first_sigmoid, first_hidden = layer_forward_step(
        earlier1, start_row, convolution_weight[0], convolution_bias[0]
    )
    second_layer = start_row + matmul(first_hidden, output_weight[0][:, :channels])
    earlier2 = from_behind(second_layer, SEQ_AXES, 1)
    second_joined, second_tanh, second_sigmoid, second_hidden = layer_forward_step(
        earlier2, second_layer, convolution_weight[1], convolution_bias[1]
    )
    past2, local2, second_conv_output, second_output, second_bias = layer_backward_step(
        second_joined,
        second_tanh,
        second_sigmoid,
        second_hidden,
        convolution_weight[1],
        output_weight[1],
        output_cotangent_rows,
        skip_cotangent_rows,
    )
    carried_state = output_cotangent_rows + local2 + from_behind(past2, SEQ_AXES, -1)
    past1, local1, first_conv_output, first_output, first_bias = layer_backward_step(
        first_joined,
        first_tanh,
        first_sigmoid,
        first_hidden,
        convolution_weight[0],
        output_weight[0],
        carried_state,
        skip_cotangent_rows,
    )
    rim_rows = from_behind(past1[:half], SEQ_AXES, -1)
    input_grad = carried_state + local1 + jnp.concatenate([past1[half:], rim_rows], axis=0)
    devices = lax.axis_size(SEQ_AXES + DP_AXES)
    factor = 1.0 / math.sqrt(rows * devices)
    conv_terms = jnp.concatenate([first_conv_output, second_conv_output], axis=0)
    out_terms = jnp.concatenate([first_output, second_output], axis=0)
    bias_terms = jnp.concatenate([first_bias, second_bias], axis=0)
    bias_cols = bias_terms.reshape(conv_terms.shape[0], -1)
    bias_cols = jnp.pad(bias_cols, ((0, 0), (0, 128 - bias_cols.shape[1])))
    packed = jnp.concatenate([owner_rows(conv_terms), owner_rows(out_terms), owner_rows(bias_cols)], axis=1)
    summed = reduce_to_owner(packed) * factor
    conv_width, out_width = conv_terms.shape[1], out_terms.shape[1]
    conv_grad = summed[:, :conv_width]
    out_grad = summed[:, conv_width : conv_width + out_width]
    bias_grad = summed[:, conv_width + out_width : conv_width + out_width + bias_terms.shape[0] // conv_terms.shape[0]]
    bias_grad = bias_grad.reshape(-1)
    return (input_grad[None], conv_grad, out_grad, bias_grad)


def solution(mesh):
    fine = jax.sharding.Mesh(mesh.devices.reshape(4, 2, 8, 2, 2), ("y", "xl", "z", "xh", "c"))
    rows_spec = P(("xh", "c"), ("y", "xl", "z"), None)
    owner = ("y", "xl", "z", "xh", "c")
    return jax.shard_map(
        local,
        mesh=fine,
        in_specs=(rows_spec, rows_spec, rows_spec, P(), P(), P()),
        out_specs=(rows_spec, P(owner, None), P(owner, None), P(owner)),
        check_vma=False,
    )
```

```python
import math

import jax
import jax.numpy as jnp
from jax import lax
from jax.sharding import PartitionSpec as P


SEQ_AXES = ("y", "xl", "z")
DP_AXES = ("xh", "c")


def reduce_rows(block, axis):
    parts = lax.axis_size(axis)
    block = block.reshape(parts, block.shape[0] // parts, block.shape[1])
    return lax.all_to_all(block, axis, 0, 0, tiled=True).sum(axis=0)


def owner_rows(terms):
    rows, width = terms.shape
    sizes = [lax.axis_size(a) for a in ("y", "xl", "z", "xh", "c")]
    return terms.reshape(*sizes, -1, width).transpose(4, 3, 1, 0, 2, 5, 6).reshape(rows, width)


def reduce_to_owner(block):
    for axis in ("c", ("xh", "xl"), "y", "z"):
        block = reduce_rows(block, axis)
    return block


def from_behind(block, axis, distance):
    devices = range(lax.axis_size(axis))
    route = [(i - distance, i) for i in devices if i - distance in devices]
    return lax.ppermute(block, axis, route)


def matmul(left, right):
    return jnp.dot(left, right, precision=lax.Precision.HIGH, preferred_element_type=jnp.float32)


def contract(left, right, left_dim, right_dim):
    return lax.dot_general(
        left,
        right,
        (((left_dim,), (right_dim,)), ((), ())),
        precision=lax.Precision.HIGH,
        preferred_element_type=jnp.float32,
    )


def layer_forward_step(earlier, values, weight, bias):
    joined = jnp.concatenate([earlier, values], axis=1)
    taps = earlier.shape[1]
    mixed = matmul(values, weight[taps:]) + matmul(earlier, weight[:taps]) + bias
    width = weight.shape[1] // 2
    tanh_part = jnp.tanh(mixed[:, :width])
    sigm_part = jax.nn.sigmoid(mixed[:, width:])
    return (joined, tanh_part, sigm_part, tanh_part * sigm_part)


def layer_backward_step(
    joined, tanh_part, sigm_part, hidden, weight, out_w, carried_state, skip_cotangent_rows
):
    channels = carried_state.shape[1]
    outer = jnp.concatenate([carried_state, skip_cotangent_rows], axis=1)
    dhidden = contract(skip_cotangent_rows, out_w[:, channels:], 1, 1)
    dhidden = dhidden + contract(carried_state, out_w[:, :channels], 1, 1)
    dfilter = dhidden * sigm_part * (1.0 - tanh_part * tanh_part)
    dgate = dhidden * tanh_part * sigm_part * (1.0 - sigm_part)
    dmixed = jnp.concatenate([dfilter, dgate], axis=1)
    out_t = contract(outer, hidden, 0, 0)
    conv_g = contract(joined, dmixed, 0, 0)
    bias_g = jnp.sum(dmixed, axis=0)
    back = contract(dmixed, weight, 1, 1)
    return (back[:, :channels], back[:, channels:], conv_g, out_t, bias_g)


def local(
    inputs, out_cotangent, skip_cotangent, convolution_weight, convolution_bias, output_weight
):
    start_row = inputs[0]
    output_cotangent_rows = out_cotangent[0]
    skip_cotangent_rows = skip_cotangent[0]
    rows, channels = start_row.shape
    half = rows // 2
    tail = from_behind(start_row[rows - half :], SEQ_AXES, 1)
    earlier1 = jnp.concatenate([tail, start_row[: rows - half]], axis=0)
    first_joined, first_tanh, first_sigmoid, first_hidden = layer_forward_step(
        earlier1, start_row, convolution_weight[0], convolution_bias[0]
    )
    second_layer = start_row + matmul(first_hidden, output_weight[0][:, :channels])
    earlier2 = from_behind(second_layer, SEQ_AXES, 1)
    second_joined, second_tanh, second_sigmoid, second_hidden = layer_forward_step(
        earlier2, second_layer, convolution_weight[1], convolution_bias[1]
    )
    past2, local2, second_conv_output, second_output, second_bias = layer_backward_step(
        second_joined,
        second_tanh,
        second_sigmoid,
        second_hidden,
        convolution_weight[1],
        output_weight[1],
        output_cotangent_rows,
        skip_cotangent_rows,
    )
    carried_state = output_cotangent_rows + local2 + from_behind(past2, SEQ_AXES, -1)
    past1, local1, first_conv_output, first_output, first_bias = layer_backward_step(
        first_joined,
        first_tanh,
        first_sigmoid,
        first_hidden,
        convolution_weight[0],
        output_weight[0],
        carried_state,
        skip_cotangent_rows,
    )
    rim_rows = from_behind(past1[:half], SEQ_AXES, -1)
    input_grad = carried_state + local1 + jnp.concatenate([past1[half:], rim_rows], axis=0)
    devices = lax.axis_size(SEQ_AXES + DP_AXES)
    factor = 1.0 / math.sqrt(rows * devices)
    conv_terms = jnp.concatenate([first_conv_output, second_conv_output], axis=0)
    out_terms = jnp.concatenate([first_output, second_output], axis=0)
    bias_terms = jnp.concatenate([first_bias, second_bias], axis=0)
    bias_cols = owner_rows(bias_terms.reshape(conv_terms.shape[0], -1))
    bias_cols = jnp.pad(bias_cols, ((0, 0), (0, 128 - bias_cols.shape[1])))
    packed = jnp.concatenate([owner_rows(conv_terms), owner_rows(out_terms), bias_cols], axis=1)
    summed = reduce_to_owner(packed) * factor
    conv_width, out_width = conv_terms.shape[1], out_terms.shape[1]
    conv_grad = summed[:, :conv_width]
    out_grad = summed[:, conv_width : conv_width + out_width]
    bias_grad = summed[:, conv_width + out_width : conv_width + out_width + bias_terms.shape[0] // conv_terms.shape[0]]
    bias_grad = bias_grad.reshape(-1)
    return (input_grad[None], conv_grad, out_grad, bias_grad)


def solution(mesh):
    fine = jax.sharding.Mesh(mesh.devices.reshape(4, 2, 8, 2, 2), ("y", "xl", "z", "xh", "c"))
    rows_spec = P(("xh", "c"), ("y", "xl", "z"), None)
    owner = ("y", "xl", "z", "xh", "c")
    return jax.shard_map(
        local,
        mesh=fine,
        in_specs=(rows_spec, rows_spec, rows_spec, P(), P(), P()),
        out_specs=(rows_spec, P(owner, None), P(owner, None), P(owner)),
        check_vma=False,
    )
```

```python
import math

import jax
import jax.numpy as jnp
from jax import lax
from jax.sharding import PartitionSpec as P


SEQ_AXES = ("y", "xl", "z")
DP_AXES = ("xh", "c")


def reduce_rows(block, axis):
    parts = lax.axis_size(axis)
    block = block.reshape(parts, block.shape[0] // parts, block.shape[1])
    return lax.all_to_all(block, axis, 0, 0, tiled=True).sum(axis=0)


def owner_rows(terms):
    rows, width = terms.shape
    sizes = [lax.axis_size(a) for a in ("y", "xl", "z", "xh", "c")]
    return terms.reshape(*sizes, -1, width).transpose(4, 0, 3, 1, 2, 5, 6).reshape(rows, width)


def reduce_to_owner(block):
    for axis in ("c", "y", ("xh", "xl"), "z"):
        block = reduce_rows(block, axis)
    return block


def from_behind(block, axis, distance):
    devices = range(lax.axis_size(axis))
    route = [(i - distance, i) for i in devices if i - distance in devices]
    return lax.ppermute(block, axis, route)


def matmul(left, right):
    return jnp.dot(left, right, precision=lax.Precision.HIGH, preferred_element_type=jnp.float32)


def contract(left, right, left_dim, right_dim):
    return lax.dot_general(
        left,
        right,
        (((left_dim,), (right_dim,)), ((), ())),
        precision=lax.Precision.HIGH,
        preferred_element_type=jnp.float32,
    )


def layer_forward_step(earlier, values, weight, bias):
    joined = jnp.concatenate([earlier, values], axis=1)
    taps = earlier.shape[1]
    mixed = matmul(values, weight[taps:]) + matmul(earlier, weight[:taps]) + bias
    width = weight.shape[1] // 2
    tanh_part = jnp.tanh(mixed[:, :width])
    sigm_part = jax.nn.sigmoid(mixed[:, width:])
    return (joined, tanh_part, sigm_part, tanh_part * sigm_part)


def layer_backward_step(
    joined, tanh_part, sigm_part, hidden, weight, out_w, carried_state, skip_cotangent_rows
):
    channels = carried_state.shape[1]
    outer = jnp.concatenate([carried_state, skip_cotangent_rows], axis=1)
    dhidden = contract(skip_cotangent_rows, out_w[:, channels:], 1, 1)
    dhidden = dhidden + contract(carried_state, out_w[:, :channels], 1, 1)
    dfilter = dhidden * sigm_part * (1.0 - tanh_part * tanh_part)
    dgate = dhidden * tanh_part * sigm_part * (1.0 - sigm_part)
    dmixed = jnp.concatenate([dfilter, dgate], axis=1)
    out_t = contract(outer, hidden, 0, 0)
    conv_g = contract(joined, dmixed, 0, 0)
    bias_g = jnp.sum(dmixed, axis=0)
    back = contract(dmixed, weight, 1, 1)
    return (back[:, :channels], back[:, channels:], conv_g, out_t, bias_g)


def local(
    inputs, out_cotangent, skip_cotangent, convolution_weight, convolution_bias, output_weight
):
    start_row = inputs[0]
    output_cotangent_rows = out_cotangent[0]
    skip_cotangent_rows = skip_cotangent[0]
    rows, channels = start_row.shape
    half = rows // 2
    tail = from_behind(start_row[rows - half :], SEQ_AXES, 1)
    earlier1 = jnp.concatenate([tail, start_row[: rows - half]], axis=0)
    first_joined, first_tanh, first_sigmoid, first_hidden = layer_forward_step(
        earlier1, start_row, convolution_weight[0], convolution_bias[0]
    )
    second_layer = start_row + matmul(first_hidden, output_weight[0][:, :channels])
    earlier2 = from_behind(second_layer, SEQ_AXES, 1)
    second_joined, second_tanh, second_sigmoid, second_hidden = layer_forward_step(
        earlier2, second_layer, convolution_weight[1], convolution_bias[1]
    )
    past2, local2, second_conv_output, second_output, second_bias = layer_backward_step(
        second_joined,
        second_tanh,
        second_sigmoid,
        second_hidden,
        convolution_weight[1],
        output_weight[1],
        output_cotangent_rows,
        skip_cotangent_rows,
    )
    carried_state = output_cotangent_rows + local2 + from_behind(past2, SEQ_AXES, -1)
    past1, local1, first_conv_output, first_output, first_bias = layer_backward_step(
        first_joined,
        first_tanh,
        first_sigmoid,
        first_hidden,
        convolution_weight[0],
        output_weight[0],
        carried_state,
        skip_cotangent_rows,
    )
    rim_rows = from_behind(past1[:half], SEQ_AXES, -1)
    input_grad = carried_state + local1 + jnp.concatenate([past1[half:], rim_rows], axis=0)
    devices = lax.axis_size(SEQ_AXES + DP_AXES)
    factor = 1.0 / math.sqrt(rows * devices)
    conv_terms = jnp.concatenate([first_conv_output, second_conv_output], axis=0)
    out_terms = jnp.concatenate([first_output, second_output], axis=0)
    bias_terms = jnp.concatenate([first_bias, second_bias], axis=0)
    bias_cols = bias_terms.reshape(conv_terms.shape[0], -1)
    bias_cols = jnp.pad(bias_cols, ((0, 0), (0, 128 - bias_cols.shape[1])))
    packed = jnp.concatenate([owner_rows(conv_terms), owner_rows(out_terms), owner_rows(bias_cols)], axis=1)
    summed = reduce_to_owner(packed) * factor
    conv_width, out_width = conv_terms.shape[1], out_terms.shape[1]
    conv_grad = summed[:, :conv_width]
    out_grad = summed[:, conv_width : conv_width + out_width]
    bias_grad = summed[:, conv_width + out_width : conv_width + out_width + bias_terms.shape[0] // conv_terms.shape[0]]
    bias_grad = bias_grad.reshape(-1)
    return (input_grad[None], conv_grad, out_grad, bias_grad)


def solution(mesh):
    fine = jax.sharding.Mesh(mesh.devices.reshape(4, 2, 8, 2, 2), ("y", "xl", "z", "xh", "c"))
    rows_spec = P(("xh", "c"), ("y", "xl", "z"), None)
    owner = ("y", "xl", "z", "xh", "c")
    return jax.shard_map(
        local,
        mesh=fine,
        in_specs=(rows_spec, rows_spec, rows_spec, P(), P(), P()),
        out_specs=(rows_spec, P(owner, None), P(owner, None), P(owner)),
        check_vma=False,
    )
```
